512 devices in a mesh: lat: 16 (over z_lo, core), lon: 32 (over y, z_hi, x).
Axes of the slice: x: 4, y: 4, z: 16 (z_hi: 2, z_lo: 8; z = z_hi * 8 + z_lo), core: 2. Of those that a mesh axis runs over, the one named last changes fastest.
Arguments:
- initial_state: float32 [16, 32, 64, 256], P('lat', 'lon'), may hold values from -6 to 6
- initial_reservoir: bfloat16 [16, 32, 64, 2048], P('lat', 'lon'), may hold values from -0.8984375 to 0.8984375
- coupling: bfloat16 [16, 32, 16, 4, 128, 128], P('lat', 'lon'), may hold values from -0.1875 to 0.1875
- input_weight: bfloat16 [16, 32, 16, 128, 128], P('lat', 'lon'), may hold values from -0.5 to 0.5
- readout: bfloat16 [16, 32, 2048, 256], P('lat', 'lon'), may hold values from -0.125 to 0.125
- intersection: int32 [16, 32, 2, 4], P('lat', 'lon'), may hold values from -1 to 7, as said below
Outputs:
- forecast: float32 [8, 16, 32, 64, 256], P(None, 'lat', 'lon')
The draws below stay inside these ranges and needn't reach their ends.
Inputs may be any that keep to these rules, and one draw needn't show every extreme that they name: `intersection`: each list holds distinct point numbers in its first slots and -1 in the rest, with one or more live slots; the north lists of band 0 and the south lists of the last band hold only -1; in longitude sector 0 every list that is not a polar one has all four slots live.
All inputs are finite; a program needn't handle non-finite values.
Results may differ from the reference program's by a relative error of at most 0.018.
Values may be sent and summed in bfloat16 or wider, within the bound.
No kernel may reach another device: no remote copies, remote signals or barrier semaphores. Data moves between devices by JAX's collectives and lax.ppermute only.
A program may use at most 64 MiB of HBM per device.

```python
import jax
import jax.numpy as jnp
import numpy as np
from jax import lax

N_RES = 2048
VARS = 32
BLOCK = 128
NCON = 4
LATR = 4
LONC = 2
OV = 4
MEMBERS = 64
STEPS = 8
PTS = 8
OUT_FEAT = 256
RES_BLOCKS = 16
IN_BLOCKS = 6
N_LAT = 16
N_LON = 32


def draw_intersection(key, part):
    count_all = N_LAT * N_LON * 2
    keys = jax.random.split(jax.random.fold_in(key, 11), count_all)
    orders = jax.vmap(lambda single: jax.random.permutation(single, PTS))(keys)
    orders = orders[:, :OV].reshape(N_LAT, N_LON, 2, OV).astype(jnp.int32)
    counts = jax.random.randint(jax.random.fold_in(key, 23), (N_LAT, N_LON, 2, 1), 1, OV + 1)
    sector = jnp.arange(N_LON, dtype=jnp.int32)[None, :, None, None]
    counts = jnp.where(sector == 0, OV, counts)
    slot = jnp.arange(OV, dtype=jnp.int32)[None, None, None, :]
    lists = jnp.where(slot < counts, orders, -1)
    band = jnp.arange(N_LAT, dtype=jnp.int32)[:, None, None, None]
    side = jnp.arange(2, dtype=jnp.int32)[None, None, :, None]
    polar = (band == 0) & (side == 0) | (band == N_LAT - 1) & (side == 1)
    return jnp.where(polar, -1, lists).astype(jnp.int32)


def levels(stream_key, shape, cuts, smallest, high):
    level = 1.0
    for dim, parts in cuts:
        heights = jax.random.uniform(jax.random.fold_in(jax.random.fold_in(stream_key, 6), dim), (parts,), jnp.float32, smallest / len(cuts), high / len(cuts))
        level = level * jnp.repeat(jnp.exp(heights), shape[dim] // parts).reshape((-1,) + (1,) * (len(shape) - 1 - dim))
    return level


def gaussian(stream_key, extent, width, limit, cuts=(), held_as=jnp.bfloat16):
    loudness = levels(stream_key, extent, cuts, -0.22, 0.18) if cuts else 1.0
    values = jax.random.normal(stream_key, extent, jnp.float32) * width * loudness
    return jnp.minimum(jnp.maximum(values, -limit), limit).astype(held_as)


def setup_inputs(seed: int = 0) -> dict:
    key_of = jax.random.split(jax.random.key(seed), 7)
    initial_state = gaussian(key_of[0], (N_LAT, N_LON, MEMBERS, OUT_FEAT), 1.0, 6.0, ((0, 16), (1, 32)), jnp.float32)
    initial_reservoir = jnp.clip(jax.random.uniform(key_of[1], (N_LAT, N_LON, MEMBERS, N_RES), jnp.float32, -0.8984375, 0.8984375) * levels(key_of[1], (N_LAT, N_LON, MEMBERS, N_RES), ((0, 16), (1, 32)), -0.4, 0.0), -0.8984375, 0.8984375).astype(jnp.bfloat16)
    coupling = gaussian(key_of[2], (N_LAT, N_LON, RES_BLOCKS, NCON, BLOCK, BLOCK), (2 * NCON * BLOCK) ** -0.5, 0.1875, ((0, 16), (1, 32)))
    input_weight = gaussian(key_of[3], (N_LAT, N_LON, RES_BLOCKS, BLOCK, BLOCK), BLOCK ** -0.5, 0.5, ((0, 16), (1, 32)))
    readout = gaussian(key_of[4], (N_LAT, N_LON, N_RES, OUT_FEAT), N_RES ** -0.5, 0.125, ((0, 16), (1, 32)))
    intersection = draw_intersection(jax.random.fold_in(key_of[6], 71), 0)
    return dict(initial_state=initial_state, initial_reservoir=initial_reservoir, coupling=coupling, input_weight=input_weight, readout=readout, intersection=intersection)


def select_points(source, lists):
    bands, sectors, members = source.shape[0], source.shape[1], source.shape[2]
    points = source.astype(jnp.float32).reshape(bands, sectors, members, PTS, VARS)
    onehot = (lists[..., None] == jnp.arange(PTS, dtype=jnp.int32)).astype(jnp.float32)
    picked = jnp.einsum('ijsp,ijmpv->ijmsv', onehot, points)
    return picked.astype(jnp.bfloat16).reshape(bands, sectors, members, OV * VARS)


def band_update(pieces):
    inputs, reservoir, coupling, input_weight, readout = pieces
    sectors, members = reservoir.shape[0], reservoir.shape[1]
    blocks = reservoir.astype(jnp.float32).reshape(sectors, members, RES_BLOCKS, BLOCK)
    linked = np.arange(RES_BLOCKS)[:, None] + np.arange(NCON)[None, :]
    linked = linked % RES_BLOCKS
    gathered = blocks[:, :, linked]
    activation = jnp.einsum('jmbki,jbkio->jmbo', gathered, coupling.astype(jnp.float32))
    chosen = inputs.astype(jnp.float32).reshape(sectors, members, IN_BLOCKS, BLOCK)
    chosen = chosen[:, :, np.arange(RES_BLOCKS) % IN_BLOCKS]
    activation = activation + jnp.einsum('jmbi,jbio->jmbo', chosen, input_weight.astype(jnp.float32))
    fresh = jnp.tanh(activation).astype(jnp.bfloat16).reshape(sectors, members, N_RES)
    widened = fresh.astype(jnp.float32)
    even_nodes = (jnp.arange(N_RES) % 2) == 0
    features = jnp.where(even_nodes, widened * widened, widened).astype(jnp.bfloat16)
    result = jnp.einsum('jmn,jny->jmy', features.astype(jnp.float32), readout.astype(jnp.float32))
    return fresh, result


def reference(initial_state, initial_reservoir, coupling, input_weight, readout, intersection):
    current = initial_state
    reservoir = initial_reservoir
    outputs = []
    for moment in range(STEPS):
        rounded = current.astype(jnp.bfloat16)
        columns = rounded.reshape(N_LAT, N_LON, MEMBERS, LONC, LATR * VARS)
        west_col = jnp.roll(columns[:, :, :, LONC - 1], 1, axis=1)
        east_col = jnp.roll(columns[:, :, :, 0], -1, axis=1)
        empty = jnp.zeros_like(rounded[:1])
        from_north = jnp.concatenate([empty, rounded[:-1]], axis=0)
        from_south = jnp.concatenate([rounded[1:], empty], axis=0)
        north_part = select_points(from_north, intersection[:, :, 0])
        south_part = select_points(from_south, intersection[:, :, 1])
        inputs = jnp.concatenate([rounded, west_col, east_col, north_part, south_part], axis=-1)
        reservoir, current = lax.map(band_update, (inputs, reservoir, coupling, input_weight, readout))
        outputs.append(current)
    return jnp.stack(outputs)
```

```python
import jax
import jax.numpy as jnp
import numpy as np
from jax import lax
from jax.experimental import pallas as pl
from jax.experimental.pallas import tpu as pltpu
from jax.sharding import PartitionSpec as P

VARS = 32
LATR = 4
LONC = 2
OV = 4
STEPS = 8
PTS = 8


def shifted(value, axis, by):
    peers = lax.axis_size(axis)
    pairs = [(i, i + by) for i in range(peers) if 0 <= i + by < peers]
    return lax.ppermute(value, axis, pairs)


def ring(value, axis, by):
    peers = lax.axis_size(axis)
    return lax.ppermute(value, axis, [(i, (i + by) % peers) for i in range(peers)])


def selector(slot_list, breadth):
    onehot = (slot_list[:, None] == jnp.arange(PTS, dtype=jnp.int32)[None, :]).astype(jnp.bfloat16)
    eye = jnp.eye(VARS, dtype=jnp.bfloat16)
    full = onehot.T[:, None, :, None] * eye[None, :, None, :]
    return full.reshape(PTS * VARS, OV * VARS)


def step_kernel(u_ref, w_ref, e_ref, n_ref, s_ref, sn_ref, ss_ref, r_ref, c_ref, win_ref, ro_ref,
                f_out, u_out, lo_out, hi_out, r_out, feat_scr):
    members, half = lo_out.shape
    res_blocks, links, breadth, _ = c_ref.shape
    u = u_ref[...]
    north = jnp.dot(n_ref[...], sn_ref[...], preferred_element_type=jnp.float32).astype(jnp.bfloat16)
    south = jnp.dot(s_ref[...], ss_ref[...], preferred_element_type=jnp.float32).astype(jnp.bfloat16)
    pieces = [u[:, j * breadth:(j + 1) * breadth] for j in range(u.shape[1] // breadth)]
    pieces += [w_ref[...], e_ref[...], north, south]
    r = r_ref[...]
    even = lax.broadcasted_iota(jnp.int32, (members, breadth), 1) % 2 == 0
    for b in range(res_blocks):
        acc = jnp.dot(pieces[b % len(pieces)], win_ref[b], preferred_element_type=jnp.float32)
        for k in range(links):
            blk = (b + k) % res_blocks
            acc = acc + jnp.dot(r[:, blk * breadth:(blk + 1) * breadth], c_ref[b, k],
                                preferred_element_type=jnp.float32)
        rb = jnp.tanh(acc).astype(jnp.bfloat16)
        r_out[:, b * breadth:(b + 1) * breadth] = rb
        wide = rb.astype(jnp.float32)
        feat_scr[:, b * breadth:(b + 1) * breadth] = jnp.where(even, wide * wide, wide).astype(jnp.bfloat16)
    f = jnp.dot(feat_scr[...], ro_ref[...], preferred_element_type=jnp.float32)
    f_out[...] = f
    ub = f.astype(jnp.bfloat16)
    u_out[...] = ub
    lo_out[...] = ub[:, :half]
    hi_out[...] = ub[:, half:]


def step_call(u, west, east, north_src, south_src, sel_n, sel_s, reservoir, block_weight, entry_weight, read_weight):
    members, feats = u.shape
    nodes = reservoir.shape[1]
    half = feats // LONC
    vmem = pltpu.MemorySpace.VMEM
    spec = pl.BlockSpec(memory_space=vmem)
    out_shape = (
        jax.ShapeDtypeStruct((members, feats), jnp.float32),
        jax.ShapeDtypeStruct((members, feats), jnp.bfloat16),
        jax.ShapeDtypeStruct((members, half), jnp.bfloat16),
        jax.ShapeDtypeStruct((members, half), jnp.bfloat16),
        jax.ShapeDtypeStruct((members, nodes), jnp.bfloat16),
    )
    return pl.pallas_call(
        step_kernel,
        out_shape=out_shape,
        in_specs=[spec] * 11,
        out_specs=tuple([spec] * 5),
        scratch_shapes=[pltpu.VMEM((members, nodes), jnp.bfloat16)],
        compiler_params=pltpu.CompilerParams(vmem_limit_bytes=32 * 1024 * 1024),
    )(u, west, east, north_src, south_src, sel_n, sel_s, reservoir, block_weight, entry_weight, read_weight)


def per_device(initial_state, initial_reservoir, coupling, input_weight, readout, intersection):
    current = initial_state[0, 0]
    reservoir = initial_reservoir[0, 0]
    block_weight = coupling[0, 0]
    entry_weight = input_weight[0, 0]
    read_weight = readout[0, 0]
    lists = intersection[0, 0]
    breadth = block_weight.shape[2]
    half = current.shape[1] // LONC
    sel_n = selector(lists[0], breadth)
    sel_s = selector(lists[1], breadth)
    rounded = current.astype(jnp.bfloat16)
    low = rounded[:, :half]
    high = rounded[:, half:]
    outputs = []
    for moment in range(STEPS):
        west = ring(high, "lon", 1)
        east = ring(low, "lon", -1)
        from_north = shifted(rounded, "lat", 1)
        from_south = shifted(rounded, "lat", -1)
        current, rounded, low, high, reservoir = step_call(
            rounded, west, east, from_north, from_south, sel_n, sel_s,
            reservoir, block_weight, entry_weight, read_weight)
        outputs.append(current)
    return jnp.stack(outputs)[:, None, None]


def solution(mesh):
    in_specs = (
        P("lat", "lon", None, None),
        P("lat", "lon", None, None),
        P("lat", "lon", None, None, None, None),
        P("lat", "lon", None, None, None),
        P("lat", "lon", None, None),
        P("lat", "lon", None, None),
    )
    out_specs = P(None, "lat", "lon", None, None)
    return jax.shard_map(
        per_device, mesh=mesh, in_specs=in_specs, out_specs=out_specs, check_vma=False
    )
```

```python
import jax
import jax.numpy as jnp
import numpy as np
from jax import lax
from jax.experimental import pallas as pl
from jax.experimental.pallas import tpu as pltpu
from jax.sharding import PartitionSpec as P

VARS = 32
LATR = 4
LONC = 2
OV = 4
STEPS = 8
PTS = 8


def selector(slot_list, breadth):
    onehot = (slot_list[:, None] == jnp.arange(PTS, dtype=jnp.int32)[None, :]).astype(jnp.bfloat16)
    eye = jnp.eye(VARS, dtype=jnp.bfloat16)
    full = onehot.T[:, None, :, None] * eye[None, :, None, :]
    return full.reshape(PTS * VARS, OV * VARS)


def step_kernel(flag_ref, u_ref, la_ref, lb_ref, ta_ref, tb_ref, sn_ref, ss_ref, r_ref, c_ref, win_ref, ro_ref,
                f_out, u_out, sa_out, sb_out, r_out, feat_scr):
    members, half = sa_out.shape
    res_blocks, links, breadth, _ = c_ref.shape
    lon_even = jnp.broadcast_to(flag_ref[0], (members, half)) == 1
    lat_even = jnp.broadcast_to(flag_ref[1], ta_ref.shape) == 1
    west = jnp.where(lon_even, lb_ref[...], la_ref[...])
    east = jnp.where(lon_even, la_ref[...], lb_ref[...])
    north_src = jnp.where(lat_even, tb_ref[...], ta_ref[...])
    south_src = jnp.where(lat_even, ta_ref[...], tb_ref[...])
    u = u_ref[...]
    north = jnp.dot(north_src, sn_ref[...], preferred_element_type=jnp.float32).astype(jnp.bfloat16)
    south = jnp.dot(south_src, ss_ref[...], preferred_element_type=jnp.float32).astype(jnp.bfloat16)
    pieces = [u[:, j * breadth:(j + 1) * breadth] for j in range(u.shape[1] // breadth)]
    pieces += [west, east, north, south]
    r = r_ref[...]
    even = lax.broadcasted_iota(jnp.int32, (members, breadth), 1) % 2 == 0
    for b in range(res_blocks):
        acc = jnp.dot(pieces[b % len(pieces)], win_ref[b], preferred_element_type=jnp.float32)
        for k in range(links):
            blk = (b + k) % res_blocks
            acc = acc + jnp.dot(r[:, blk * breadth:(blk + 1) * breadth], c_ref[b, k],
                                preferred_element_type=jnp.float32)
        rb = jnp.tanh(acc).astype(jnp.bfloat16)
        r_out[:, b * breadth:(b + 1) * breadth] = rb
        wide = rb.astype(jnp.float32)
        feat_scr[:, b * breadth:(b + 1) * breadth] = jnp.where(even, wide * wide, wide).astype(jnp.bfloat16)
    f = jnp.dot(feat_scr[...], ro_ref[...], preferred_element_type=jnp.float32)
    f_out[...] = f
    ub = f.astype(jnp.bfloat16)
    u_out[...] = ub
    lo = ub[:, :half]
    hi = ub[:, half:]
    sa_out[...] = jnp.where(lon_even, hi, lo)
    sb_out[...] = jnp.where(lon_even, lo, hi)


def step_call(flags, u, lon_a, lon_b, lat_a, lat_b, sel_n, sel_s, reservoir, block_weight, entry_weight, read_weight):
    members, feats = u.shape
    nodes = reservoir.shape[1]
    half = feats // LONC
    spec = pl.BlockSpec(memory_space=pltpu.MemorySpace.VMEM)
    out_shape = (
        jax.ShapeDtypeStruct((members, feats), jnp.float32),
        jax.ShapeDtypeStruct((members, feats), jnp.bfloat16),
        jax.ShapeDtypeStruct((members, half), jnp.bfloat16),
        jax.ShapeDtypeStruct((members, half), jnp.bfloat16),
        jax.ShapeDtypeStruct((members, nodes), jnp.bfloat16),
    )
    return pl.pallas_call(
        step_kernel,
        out_shape=out_shape,
        in_specs=[pl.BlockSpec(memory_space=pltpu.MemorySpace.SMEM)] + [spec] * 11,
        out_specs=tuple([spec] * 5),
        scratch_shapes=[pltpu.VMEM((members, nodes), jnp.bfloat16)],
        compiler_params=pltpu.CompilerParams(vmem_limit_bytes=32 * 1024 * 1024),
    )(flags, u, lon_a, lon_b, lat_a, lat_b, sel_n, sel_s, reservoir, block_weight, entry_weight, read_weight)


def swaps(peers, odd_first, wrap):
    pairs = []
    for i in range(peers):
        partner = i + 1 if (i % 2 == 1) == odd_first else i - 1
        if wrap:
            partner %= peers
        if 0 <= partner < peers:
            pairs.append((i, partner))
    return pairs


def per_device(initial_state, initial_reservoir, coupling, input_weight, readout, intersection):
    current = initial_state[0, 0]
    reservoir = initial_reservoir[0, 0]
    block_weight = coupling[0, 0]
    entry_weight = input_weight[0, 0]
    read_weight = readout[0, 0]
    lists = intersection[0, 0]
    breadth = block_weight.shape[2]
    half = current.shape[1] // LONC
    sel_n = selector(lists[0], breadth)
    sel_s = selector(lists[1], breadth)
    lon_even = (lax.axis_index("lon") % 2 == 0).astype(jnp.int32)
    lat_even = (lax.axis_index("lat") % 2 == 0).astype(jnp.int32)
    flags = jnp.stack([lon_even, lat_even])
    lon_peers = lax.axis_size("lon")
    lat_peers = lax.axis_size("lat")
    lon_pairs_a = swaps(lon_peers, False, True)
    lon_pairs_b = swaps(lon_peers, True, True)
    lat_pairs_a = swaps(lat_peers, False, False)
    lat_pairs_b = swaps(lat_peers, True, False)
    rounded = current.astype(jnp.bfloat16)
    low = rounded[:, :half]
    high = rounded[:, half:]
    send_a = jnp.where(lon_even == 1, high, low)
    send_b = jnp.where(lon_even == 1, low, high)
    outputs = []
    for moment in range(STEPS):
        lon_b = lax.ppermute(send_b, "lon", lon_pairs_b)
        lon_a = lax.ppermute(send_a, "lon", lon_pairs_a)
        lat_b = lax.ppermute(rounded, "lat", lat_pairs_b)
        lat_a = lax.ppermute(rounded, "lat", lat_pairs_a)
        current, rounded, send_a, send_b, reservoir = step_call(
            flags, rounded, lon_a, lon_b, lat_a, lat_b, sel_n, sel_s,
            reservoir, block_weight, entry_weight, read_weight)
        outputs.append(current)
    return jnp.stack(outputs)[:, None, None]


def solution(mesh):
    in_specs = (
        P("lat", "lon", None, None),
        P("lat", "lon", None, None),
        P("lat", "lon", None, None, None, None),
        P("lat", "lon", None, None, None),
        P("lat", "lon", None, None),
        P("lat", "lon", None, None),
    )
    out_specs = P(None, "lat", "lon", None, None)
    return jax.shard_map(
        per_device, mesh=mesh, in_specs=in_specs, out_specs=out_specs, check_vma=False
    )
```

```python
import jax
import jax.numpy as jnp
from jax import lax
from jax.experimental import pallas as pl
from jax.experimental.pallas import tpu as pltpu
from jax.sharding import PartitionSpec as P


VARS = 32
LONC = 2
OV = 4
STEPS = 8
PTS = 8


def selector(slot_list):
    onehot = (slot_list[:, None] == jnp.arange(PTS, dtype=jnp.int32)[None, :]).astype(jnp.bfloat16)
    eye = jnp.eye(VARS, dtype=jnp.bfloat16)
    full = onehot.T[:, None, :, None] * eye[None, :, None, :]
    return full.reshape(PTS * VARS, OV * VARS)


def step_kernel(flag_ref, u_ref, la_ref, lb_ref, ta_ref, tb_ref, sn_ref, ss_ref, r_ref, c_ref, win_ref, ro_ref,
                f_out, u_out, sa_out, sb_out, r_out, feat_scr):
    members, half = sa_out.shape
    res_blocks, links, breadth, _ = c_ref.shape
    lon_even = jnp.broadcast_to(flag_ref[0], (members, half)) == 1
    lat_even = jnp.broadcast_to(flag_ref[1], ta_ref.shape) == 1
    west = jnp.where(lon_even, lb_ref[...], la_ref[...])
    east = jnp.where(lon_even, la_ref[...], lb_ref[...])
    north_src = jnp.where(lat_even, tb_ref[...], ta_ref[...])
    south_src = jnp.where(lat_even, ta_ref[...], tb_ref[...])
    u = u_ref[...]
    north = jnp.dot(north_src, sn_ref[...], preferred_element_type=jnp.float32).astype(jnp.bfloat16)
    south = jnp.dot(south_src, ss_ref[...], preferred_element_type=jnp.float32).astype(jnp.bfloat16)
    pieces = [u[:, j * breadth:(j + 1) * breadth] for j in range(u.shape[1] // breadth)]
    pieces += [west, east, north, south]
    r = r_ref[...]
    even = lax.broadcasted_iota(jnp.int32, (members, breadth), 1) % 2 == 0
    for b in range(res_blocks):
        acc = jnp.dot(pieces[b % len(pieces)], win_ref[b], preferred_element_type=jnp.float32)
        for k in range(links):
            blk = (b + k) % res_blocks
            acc = acc + jnp.dot(r[:, blk * breadth:(blk + 1) * breadth], c_ref[b, k],
                                preferred_element_type=jnp.float32)
        rb = jnp.tanh(acc).astype(jnp.bfloat16)
        r_out[:, b * breadth:(b + 1) * breadth] = rb
        wide = rb.astype(jnp.float32)
        feat_scr[:, b * breadth:(b + 1) * breadth] = jnp.where(even, wide * wide, wide).astype(jnp.bfloat16)
    f = jnp.dot(feat_scr[...], ro_ref[...], preferred_element_type=jnp.float32)
    f_out[...] = f
    ub = f.astype(jnp.bfloat16)
    u_out[...] = ub
    lo = ub[:, :half]
    hi = ub[:, half:]
    sa_out[...] = jnp.where(lon_even, hi, lo)
    sb_out[...] = jnp.where(lon_even, lo, hi)


def step_call(flags, u, lon_a, lon_b, lat_a, lat_b, sel_n, sel_s, reservoir, block_weight, entry_weight, read_weight):
    members, feats = u.shape
    nodes = reservoir.shape[1]
    half = feats // LONC
    spec = pl.BlockSpec(memory_space=pltpu.MemorySpace.VMEM)
    out_shape = (
        jax.ShapeDtypeStruct((members, feats), jnp.float32),
        jax.ShapeDtypeStruct((members, feats), jnp.bfloat16),
        jax.ShapeDtypeStruct((members, half), jnp.bfloat16),
        jax.ShapeDtypeStruct((members, half), jnp.bfloat16),
        jax.ShapeDtypeStruct((members, nodes), jnp.bfloat16),
    )
    return pl.pallas_call(
        step_kernel,
        out_shape=out_shape,
        in_specs=[pl.BlockSpec(memory_space=pltpu.MemorySpace.SMEM)] + [spec] * 11,
        out_specs=tuple([spec] * 5),
        scratch_shapes=[pltpu.VMEM((members, nodes), jnp.bfloat16)],
        compiler_params=pltpu.CompilerParams(vmem_limit_bytes=32 * 1024 * 1024),
    )(flags, u, lon_a, lon_b, lat_a, lat_b, sel_n, sel_s, reservoir, block_weight, entry_weight, read_weight)


def swaps(peers, odd_first, wrap):
    pairs = []
    for i in range(peers):
        partner = i + 1 if (i % 2 == 1) == odd_first else i - 1
        if wrap:
            partner %= peers
        if 0 <= partner < peers:
            pairs.append((i, partner))
    return pairs


def per_device(initial_state, initial_reservoir, coupling, input_weight, readout, intersection):
    current = initial_state[0, 0]
    reservoir = initial_reservoir[0, 0]
    block_weight = coupling[0, 0]
    entry_weight = input_weight[0, 0]
    read_weight = readout[0, 0]
    lists = intersection[0, 0]
    half = current.shape[1] // LONC
    sel_n = selector(lists[0])
    sel_s = selector(lists[1])
    lon_even = (lax.axis_index("lon") % 2 == 0).astype(jnp.int32)
    lat_even = (lax.axis_index("lat") % 2 == 0).astype(jnp.int32)
    flags = jnp.stack([lon_even, lat_even])
    lon_peers = lax.axis_size("lon")
    lat_peers = lax.axis_size("lat")
    lon_pairs_a = swaps(lon_peers, False, True)
    lon_pairs_b = swaps(lon_peers, True, True)
    lat_pairs_a = swaps(lat_peers, False, False)
    lat_pairs_b = swaps(lat_peers, True, False)
    rounded = current.astype(jnp.bfloat16)
    low = rounded[:, :half]
    high = rounded[:, half:]
    send_a = jnp.where(lon_even == 1, high, low)
    send_b = jnp.where(lon_even == 1, low, high)
    outputs = []
    for _ in range(STEPS):
        lon_b = lax.ppermute(send_b, "lon", lon_pairs_b)
        lon_a = lax.ppermute(send_a, "lon", lon_pairs_a)
        lat_b = lax.ppermute(rounded, "lat", lat_pairs_b)
        lat_a = lax.ppermute(rounded, "lat", lat_pairs_a)
        current, rounded, send_a, send_b, reservoir = step_call(
            flags, rounded, lon_a, lon_b, lat_a, lat_b, sel_n, sel_s,
            reservoir, block_weight, entry_weight, read_weight)
        outputs.append(current)
    return jnp.stack(outputs)[:, None, None]


def solution(mesh):
    in_specs = (
        P("lat", "lon", None, None),
        P("lat", "lon", None, None),
        P("lat", "lon", None, None, None, None),
        P("lat", "lon", None, None, None),
        P("lat", "lon", None, None),
        P("lat", "lon", None, None),
    )
    out_specs = P(None, "lat", "lon", None, None)
    return jax.shard_map(
        per_device, mesh=mesh, in_specs=in_specs, out_specs=out_specs, check_vma=False
    )
```

```python
import jax
import jax.numpy as jnp
from jax import lax
from jax.experimental import pallas as pl
from jax.experimental.pallas import tpu as pltpu
from jax.sharding import PartitionSpec as P


VARS = 32
LONC = 2
OV = 4
STEPS = 8
PTS = 8
IN_BLOCKS = 6


def selector(slot_list):
    onehot = (slot_list[:, None] == jnp.arange(PTS, dtype=jnp.int32)[None, :]).astype(jnp.bfloat16)
    eye = jnp.eye(VARS, dtype=jnp.bfloat16)
    full = onehot.T[:, None, :, None] * eye[None, :, None, :]
    return full.reshape(PTS * VARS, OV * VARS)


def couple_kernel(u_ref, r_ref, c_ref, win_ref, acc_out):
    res_blocks, links, breadth, _ = c_ref.shape
    u = u_ref[...]
    own = u.shape[1] // breadth
    r = r_ref[...]
    for b in range(res_blocks):
        acc = jnp.zeros((r.shape[0], breadth), jnp.float32)
        if b % IN_BLOCKS < own:
            j = b % IN_BLOCKS
            acc = jnp.dot(u[:, j * breadth:(j + 1) * breadth], win_ref[b], preferred_element_type=jnp.float32)
        for k in range(links):
            blk = (b + k) % res_blocks
            acc = acc + jnp.dot(r[:, blk * breadth:(blk + 1) * breadth], c_ref[b, k],
                                preferred_element_type=jnp.float32)
        acc_out[:, b * breadth:(b + 1) * breadth] = acc


def step_kernel(flag_ref, acc_ref, la_ref, lb_ref, ta_ref, tb_ref, sn_ref, ss_ref, win_ref, ro_ref,
                f_out, u_out, sa_out, sb_out, r_out, feat_scr):
    members, half = sa_out.shape
    res_blocks, breadth, _ = win_ref.shape
    lon_even = jnp.broadcast_to(flag_ref[0], (members, half)) == 1
    lat_even = jnp.broadcast_to(flag_ref[1], ta_ref.shape) == 1
    west = jnp.where(lon_even, lb_ref[...], la_ref[...])
    east = jnp.where(lon_even, la_ref[...], lb_ref[...])
    north_src = jnp.where(lat_even, tb_ref[...], ta_ref[...])
    south_src = jnp.where(lat_even, ta_ref[...], tb_ref[...])
    north = jnp.dot(north_src, sn_ref[...], preferred_element_type=jnp.float32).astype(jnp.bfloat16)
    south = jnp.dot(south_src, ss_ref[...], preferred_element_type=jnp.float32).astype(jnp.bfloat16)
    pieces = [west, east, north, south]
    own = IN_BLOCKS - len(pieces)
    even = lax.broadcasted_iota(jnp.int32, (members, breadth), 1) % 2 == 0
    for b in range(res_blocks):
        acc = acc_ref[:, b * breadth:(b + 1) * breadth]
        if b % IN_BLOCKS >= own:
            acc = acc + jnp.dot(pieces[b % IN_BLOCKS - own], win_ref[b], preferred_element_type=jnp.float32)
        rb = jnp.tanh(acc).astype(jnp.bfloat16)
        r_out[:, b * breadth:(b + 1) * breadth] = rb
        wide = rb.astype(jnp.float32)
        feat_scr[:, b * breadth:(b + 1) * breadth] = jnp.where(even, wide * wide, wide).astype(jnp.bfloat16)
    f = jnp.dot(feat_scr[...], ro_ref[...], preferred_element_type=jnp.float32)
    f_out[...] = f
    ub = f.astype(jnp.bfloat16)
    u_out[...] = ub
    lo = ub[:, :half]
    hi = ub[:, half:]
    sa_out[...] = jnp.where(lon_even, hi, lo)
    sb_out[...] = jnp.where(lon_even, lo, hi)


VMEM_SPEC = pl.BlockSpec(memory_space=pltpu.MemorySpace.VMEM)


def couple_call(u, reservoir, block_weight, entry_weight):
    members, nodes = reservoir.shape
    return pl.pallas_call(
        couple_kernel,
        out_shape=jax.ShapeDtypeStruct((members, nodes), jnp.float32),
        in_specs=[VMEM_SPEC] * 4,
        out_specs=VMEM_SPEC,
        compiler_params=pltpu.CompilerParams(vmem_limit_bytes=32 * 1024 * 1024),
    )(u, reservoir, block_weight, entry_weight)


def step_call(flags, acc, lon_a, lon_b, lat_a, lat_b, sel_n, sel_s, entry_weight, read_weight):
    members, nodes = acc.shape
    feats = read_weight.shape[1]
    half = feats // LONC
    out_shape = (
        jax.ShapeDtypeStruct((members, feats), jnp.float32),
        jax.ShapeDtypeStruct((members, feats), jnp.bfloat16),
        jax.ShapeDtypeStruct((members, half), jnp.bfloat16),
        jax.ShapeDtypeStruct((members, half), jnp.bfloat16),
        jax.ShapeDtypeStruct((members, nodes), jnp.bfloat16),
    )
    return pl.pallas_call(
        step_kernel,
        out_shape=out_shape,
        in_specs=[pl.BlockSpec(memory_space=pltpu.MemorySpace.SMEM)] + [VMEM_SPEC] * 9,
        out_specs=tuple([VMEM_SPEC] * 5),
        scratch_shapes=[pltpu.VMEM((members, nodes), jnp.bfloat16)],
        compiler_params=pltpu.CompilerParams(vmem_limit_bytes=32 * 1024 * 1024),
    )(flags, acc, lon_a, lon_b, lat_a, lat_b, sel_n, sel_s, entry_weight, read_weight)


def swaps(peers, odd_first, wrap):
    pairs = []
    for i in range(peers):
        partner = i + 1 if (i % 2 == 1) == odd_first else i - 1
        if wrap:
            partner %= peers
        if 0 <= partner < peers:
            pairs.append((i, partner))
    return pairs


def per_device(initial_state, initial_reservoir, coupling, input_weight, readout, intersection):
    current = initial_state[0, 0]
    reservoir = initial_reservoir[0, 0]
    block_weight = coupling[0, 0]
    entry_weight = input_weight[0, 0]
    read_weight = readout[0, 0]
    lists = intersection[0, 0]
    half = current.shape[1] // LONC
    sel_n = selector(lists[0])
    sel_s = selector(lists[1])
    lon_even = (lax.axis_index("lon") % 2 == 0).astype(jnp.int32)
    lat_even = (lax.axis_index("lat") % 2 == 0).astype(jnp.int32)
    flags = jnp.stack([lon_even, lat_even])
    lon_peers = lax.axis_size("lon")
    lat_peers = lax.axis_size("lat")
    lon_pairs_a = swaps(lon_peers, False, True)
    lon_pairs_b = swaps(lon_peers, True, True)
    lat_pairs_a = swaps(lat_peers, False, False)
    lat_pairs_b = swaps(lat_peers, True, False)
    rounded = current.astype(jnp.bfloat16)
    low = rounded[:, :half]
    high = rounded[:, half:]
    send_a = jnp.where(lon_even == 1, high, low)
    send_b = jnp.where(lon_even == 1, low, high)
    outputs = []
    for _ in range(STEPS):
        lon_b = lax.ppermute(send_b, "lon", lon_pairs_b)
        lon_a = lax.ppermute(send_a, "lon", lon_pairs_a)
        lat_b = lax.ppermute(rounded, "lat", lat_pairs_b)
        lat_a = lax.ppermute(rounded, "lat", lat_pairs_a)
        acc = couple_call(rounded, reservoir, block_weight, entry_weight)
        current, rounded, send_a, send_b, reservoir = step_call(
            flags, acc, lon_a, lon_b, lat_a, lat_b, sel_n, sel_s, entry_weight, read_weight)
        outputs.append(current)
    return jnp.stack(outputs)[:, None, None]


def solution(mesh):
    in_specs = (
        P("lat", "lon", None, None),
        P("lat", "lon", None, None),
        P("lat", "lon", None, None, None, None),
        P("lat", "lon", None, None, None),
        P("lat", "lon", None, None),
        P("lat", "lon", None, None),
    )
    out_specs = P(None, "lat", "lon", None, None)
    return jax.shard_map(
        per_device, mesh=mesh, in_specs=in_specs, out_specs=out_specs, check_vma=False
    )
```

```python
import jax
import jax.numpy as jnp
from jax import lax
from jax.experimental import pallas as pl
from jax.experimental.pallas import tpu as pltpu
from jax.sharding import PartitionSpec as P


VARS = 32
LONC = 2
OV = 4
STEPS = 8
PTS = 8
IN_BLOCKS = 6


def selector(slot_list):
    onehot = (slot_list[:, None] == jnp.arange(PTS, dtype=jnp.int32)[None, :]).astype(jnp.bfloat16)
    eye = jnp.eye(VARS, dtype=jnp.bfloat16)
    full = onehot.T[:, None, :, None] * eye[None, :, None, :]
    return full.reshape(PTS * VARS, OV * VARS)


def lon_blocks(res_blocks):
    return [b for b in range(res_blocks) if b % IN_BLOCKS in (2, 3)]


def spans(blocks):
    runs = []
    for b in blocks:
        if runs and runs[-1][0] + runs[-1][1] == b:
            runs[-1] = (runs[-1][0], runs[-1][1] + 1)
        else:
            runs.append((b, 1))
    return runs


def couple_kernel(flag_ref, u_ref, ta_ref, tb_ref, sn_ref, ss_ref, r_ref, c_ref, win_ref, ro_ref,
                  acc_out, r_out, f_out, feat_scr):
    res_blocks, links, breadth, _ = c_ref.shape
    members = r_ref.shape[0]
    lat_even = jnp.broadcast_to(flag_ref[1], ta_ref.shape) == 1
    north_src = jnp.where(lat_even, tb_ref[...], ta_ref[...])
    south_src = jnp.where(lat_even, ta_ref[...], tb_ref[...])
    north = jnp.dot(north_src, sn_ref[...], preferred_element_type=jnp.float32).astype(jnp.bfloat16)
    south = jnp.dot(south_src, ss_ref[...], preferred_element_type=jnp.float32).astype(jnp.bfloat16)
    u = u_ref[...]
    pieces = {0: u[:, :breadth], 1: u[:, breadth:2 * breadth], 4: north, 5: south}
    r = r_ref[...]
    even = lax.broadcasted_iota(jnp.int32, (members, breadth), 1) % 2 == 0
    later = lon_blocks(res_blocks)
    for b in range(res_blocks):
        acc = jnp.zeros((members, breadth), jnp.float32)
        if b % IN_BLOCKS in pieces:
            acc = jnp.dot(pieces[b % IN_BLOCKS], win_ref[b], preferred_element_type=jnp.float32)
        for k in range(links):
            blk = (b + k) % res_blocks
            acc = acc + jnp.dot(r[:, blk * breadth:(blk + 1) * breadth], c_ref[b, k],
                                preferred_element_type=jnp.float32)
        if b in later:
            i = later.index(b)
            acc_out[:, i * breadth:(i + 1) * breadth] = acc
        else:
            rb = jnp.tanh(acc).astype(jnp.bfloat16)
            r_out[:, b * breadth:(b + 1) * breadth] = rb
            wide = rb.astype(jnp.float32)
            feat_scr[:, b * breadth:(b + 1) * breadth] = jnp.where(even, wide * wide, wide).astype(jnp.bfloat16)
    f = jnp.zeros(f_out.shape, jnp.float32)
    for first, count in spans([b for b in range(res_blocks) if b not in later]):
        rows = slice(first * breadth, (first + count) * breadth)
        f = f + jnp.dot(feat_scr[:, rows], ro_ref[rows, :], preferred_element_type=jnp.float32)
    f_out[...] = f


def step_kernel(flag_ref, acc_ref, la_ref, lb_ref, win_ref, ro_ref, rp_ref, fp_ref,
                f_out, u_out, sa_out, sb_out, r_out, feat_scr):
    members, half = sa_out.shape
    res_blocks, breadth, _ = win_ref.shape
    lon_even = jnp.broadcast_to(flag_ref[0], (members, half)) == 1
    west = jnp.where(lon_even, lb_ref[...], la_ref[...])
    east = jnp.where(lon_even, la_ref[...], lb_ref[...])
    pieces = {2: west, 3: east}
    even = lax.broadcasted_iota(jnp.int32, (members, breadth), 1) % 2 == 0
    later = lon_blocks(res_blocks)
    r_out[...] = rp_ref[...]
    for i, b in enumerate(later):
        acc = acc_ref[:, i * breadth:(i + 1) * breadth]
        acc = acc + jnp.dot(pieces[b % IN_BLOCKS], win_ref[b], preferred_element_type=jnp.float32)
        rb = jnp.tanh(acc).astype(jnp.bfloat16)
        r_out[:, b * breadth:(b + 1) * breadth] = rb
        wide = rb.astype(jnp.float32)
        feat_scr[:, i * breadth:(i + 1) * breadth] = jnp.where(even, wide * wide, wide).astype(jnp.bfloat16)
    f = fp_ref[...]
    done = 0
    for first, count in spans(later):
        rows = slice(first * breadth, (first + count) * breadth)
        f = f + jnp.dot(feat_scr[:, done * breadth:(done + count) * breadth], ro_ref[rows, :],
                        preferred_element_type=jnp.float32)
        done += count
    f_out[...] = f
    ub = f.astype(jnp.bfloat16)
    u_out[...] = ub
    lo = ub[:, :half]
    hi = ub[:, half:]
    sa_out[...] = jnp.where(lon_even, hi, lo)
    sb_out[...] = jnp.where(lon_even, lo, hi)


VMEM_SPEC = pl.BlockSpec(memory_space=pltpu.MemorySpace.VMEM)
SMEM_SPEC = pl.BlockSpec(memory_space=pltpu.MemorySpace.SMEM)
PARAMS = pltpu.CompilerParams(vmem_limit_bytes=32 * 1024 * 1024)


def couple_call(flags, u, lat_a, lat_b, sel_n, sel_s, reservoir, block_weight, entry_weight, read_weight):
    members, nodes = reservoir.shape
    breadth = block_weight.shape[2]
    later = len(lon_blocks(block_weight.shape[0]))
    out_shape = (
        jax.ShapeDtypeStruct((members, later * breadth), jnp.float32),
        jax.ShapeDtypeStruct((members, nodes), jnp.bfloat16),
        jax.ShapeDtypeStruct((members, read_weight.shape[1]), jnp.float32),
    )
    return pl.pallas_call(
        couple_kernel,
        out_shape=out_shape,
        in_specs=[SMEM_SPEC] + [VMEM_SPEC] * 9,
        out_specs=tuple([VMEM_SPEC] * 3),
        scratch_shapes=[pltpu.VMEM((members, nodes), jnp.bfloat16)],
        compiler_params=PARAMS,
    )(flags, u, lat_a, lat_b, sel_n, sel_s, reservoir, block_weight, entry_weight, read_weight)


def step_call(flags, acc, lon_a, lon_b, entry_weight, read_weight, r_part, f_part):
    members, nodes = r_part.shape
    feats = read_weight.shape[1]
    half = feats // LONC
    out_shape = (
        jax.ShapeDtypeStruct((members, feats), jnp.float32),
        jax.ShapeDtypeStruct((members, feats), jnp.bfloat16),
        jax.ShapeDtypeStruct((members, half), jnp.bfloat16),
        jax.ShapeDtypeStruct((members, half), jnp.bfloat16),
        jax.ShapeDtypeStruct((members, nodes), jnp.bfloat16),
    )
    return pl.pallas_call(
        step_kernel,
        out_shape=out_shape,
        in_specs=[SMEM_SPEC] + [VMEM_SPEC] * 7,
        out_specs=tuple([VMEM_SPEC] * 5),
        scratch_shapes=[pltpu.VMEM(acc.shape, jnp.bfloat16)],
        compiler_params=PARAMS,
    )(flags, acc, lon_a, lon_b, entry_weight, read_weight, r_part, f_part)


def swaps(peers, odd_first, wrap):
    pairs = []
    for i in range(peers):
        partner = i + 1 if (i % 2 == 1) == odd_first else i - 1
        if wrap:
            partner %= peers
        if 0 <= partner < peers:
            pairs.append((i, partner))
    return pairs


def per_device(initial_state, initial_reservoir, coupling, input_weight, readout, intersection):
    current = initial_state[0, 0]
    reservoir = initial_reservoir[0, 0]
    block_weight = coupling[0, 0]
    entry_weight = input_weight[0, 0]
    read_weight = readout[0, 0]
    lists = intersection[0, 0]
    half = current.shape[1] // LONC
    sel_n = selector(lists[0])
    sel_s = selector(lists[1])
    lon_even = (lax.axis_index("lon") % 2 == 0).astype(jnp.int32)
    lat_even = (lax.axis_index("lat") % 2 == 0).astype(jnp.int32)
    flags = jnp.stack([lon_even, lat_even])
    lon_peers = lax.axis_size("lon")
    lat_peers = lax.axis_size("lat")
    lon_pairs_a = swaps(lon_peers, False, True)
    lon_pairs_b = swaps(lon_peers, True, True)
    lat_pairs_a = swaps(lat_peers, False, False)
    lat_pairs_b = swaps(lat_peers, True, False)
    rounded = current.astype(jnp.bfloat16)
    low = rounded[:, :half]
    high = rounded[:, half:]
    send_a = jnp.where(lon_even == 1, high, low)
    send_b = jnp.where(lon_even == 1, low, high)
    outputs = []
    for _ in range(STEPS):
        lon_b = lax.ppermute(send_b, "lon", lon_pairs_b)
        lon_a = lax.ppermute(send_a, "lon", lon_pairs_a)
        lat_b = lax.ppermute(rounded, "lat", lat_pairs_b)
        lat_a = lax.ppermute(rounded, "lat", lat_pairs_a)
        acc, r_part, f_part = couple_call(flags, rounded, lat_a, lat_b, sel_n, sel_s,
                                          reservoir, block_weight, entry_weight, read_weight)
        current, rounded, send_a, send_b, reservoir = step_call(
            flags, acc, lon_a, lon_b, entry_weight, read_weight, r_part, f_part)
        outputs.append(current)
    return jnp.stack(outputs)[:, None, None]


def solution(mesh):
    in_specs = (
        P("lat", "lon", None, None),
        P("lat", "lon", None, None),
        P("lat", "lon", None, None, None, None),
        P("lat", "lon", None, None, None),
        P("lat", "lon", None, None),
        P("lat", "lon", None, None),
    )
    out_specs = P(None, "lat", "lon", None, None)
    return jax.shard_map(
        per_device, mesh=mesh, in_specs=in_specs, out_specs=out_specs, check_vma=False
    )
```

```python
import jax
import jax.numpy as jnp
from jax import lax
from jax.experimental import pallas as pl
from jax.experimental.pallas import tpu as pltpu
from jax.sharding import PartitionSpec as P


VARS = 32
LONC = 2
OV = 4
STEPS = 8
IN_BLOCKS = 6


def build_selector(lists_ref, side, shape):
    row = lax.broadcasted_iota(jnp.int32, shape, 0)
    col = lax.broadcasted_iota(jnp.int32, shape, 1)
    slot = col // VARS
    wanted = jnp.full(shape, lists_ref[side, OV - 1], jnp.int32)
    for s in range(OV - 2, -1, -1):
        wanted = jnp.where(slot == s, lists_ref[side, s], wanted)
    hit = (row // VARS == wanted) & (row % VARS == col % VARS)
    return hit.astype(jnp.bfloat16)


def couple_kernel(lists_ref, u_ref, r_ref, c_ref, win_ref, acc_out, sn_out, ss_out):
    res_blocks, links, breadth, _ = c_ref.shape
    sn_out[...] = build_selector(lists_ref, 0, sn_out.shape)
    ss_out[...] = build_selector(lists_ref, 1, ss_out.shape)
    u = u_ref[...]
    own = u.shape[1] // breadth
    r = r_ref[...]
    for b in range(res_blocks):
        acc = jnp.zeros((r.shape[0], breadth), jnp.float32)
        if b % IN_BLOCKS < own:
            j = b % IN_BLOCKS
            acc = jnp.dot(u[:, j * breadth:(j + 1) * breadth], win_ref[b], preferred_element_type=jnp.float32)
        for k in range(links):
            blk = (b + k) % res_blocks
            acc = acc + jnp.dot(r[:, blk * breadth:(blk + 1) * breadth], c_ref[b, k],
                                preferred_element_type=jnp.float32)
        acc_out[:, b * breadth:(b + 1) * breadth] = acc


def step_kernel(flag_ref, acc_ref, la_ref, lb_ref, ta_ref, tb_ref, sn_ref, ss_ref, win_ref, ro_ref,
                f_out, u_out, sa_out, sb_out, r_out, feat_scr):
    members, half = sa_out.shape
    res_blocks, breadth, _ = win_ref.shape
    lon_even = jnp.broadcast_to(flag_ref[0], (members, half)) == 1
    lat_even = jnp.broadcast_to(flag_ref[1], ta_ref.shape) == 1
    west = jnp.where(lon_even, lb_ref[...], la_ref[...])
    east = jnp.where(lon_even, la_ref[...], lb_ref[...])
    north_src = jnp.where(lat_even, tb_ref[...], ta_ref[...])
    south_src = jnp.where(lat_even, ta_ref[...], tb_ref[...])
    north = jnp.dot(north_src, sn_ref[...], preferred_element_type=jnp.float32).astype(jnp.bfloat16)
    south = jnp.dot(south_src, ss_ref[...], preferred_element_type=jnp.float32).astype(jnp.bfloat16)
    pieces = [west, east, north, south]
    own = IN_BLOCKS - len(pieces)
    even = lax.broadcasted_iota(jnp.int32, (members, breadth), 1) % 2 == 0
    for b in range(res_blocks):
        acc = acc_ref[:, b * breadth:(b + 1) * breadth]
        if b % IN_BLOCKS >= own:
            acc = acc + jnp.dot(pieces[b % IN_BLOCKS - own], win_ref[b], preferred_element_type=jnp.float32)
        rb = jnp.tanh(acc).astype(jnp.bfloat16)
        r_out[:, b * breadth:(b + 1) * breadth] = rb
        wide = rb.astype(jnp.float32)
        feat_scr[:, b * breadth:(b + 1) * breadth] = jnp.where(even, wide * wide, wide).astype(jnp.bfloat16)
    f = jnp.dot(feat_scr[...], ro_ref[...], preferred_element_type=jnp.float32)
    f_out[...] = f
    ub = f.astype(jnp.bfloat16)
    u_out[...] = ub
    lo = ub[:, :half]
    hi = ub[:, half:]
    sa_out[...] = jnp.where(lon_even, hi, lo)
    sb_out[...] = jnp.where(lon_even, lo, hi)


VMEM_SPEC = pl.BlockSpec(memory_space=pltpu.MemorySpace.VMEM)


def couple_call(lists, u, reservoir, block_weight, entry_weight):
    members, nodes = reservoir.shape
    feats = u.shape[1]
    picked = OV * VARS
    out_shape = (
        jax.ShapeDtypeStruct((members, nodes), jnp.float32),
        jax.ShapeDtypeStruct((feats, picked), jnp.bfloat16),
        jax.ShapeDtypeStruct((feats, picked), jnp.bfloat16),
    )
    return pl.pallas_call(
        couple_kernel,
        out_shape=out_shape,
        in_specs=[pl.BlockSpec(memory_space=pltpu.MemorySpace.SMEM)] + [VMEM_SPEC] * 4,
        out_specs=(VMEM_SPEC, VMEM_SPEC, VMEM_SPEC),
        compiler_params=pltpu.CompilerParams(vmem_limit_bytes=32 * 1024 * 1024),
    )(lists, u, reservoir, block_weight, entry_weight)


def step_call(flags, acc, lon_a, lon_b, lat_a, lat_b, sel_n, sel_s, entry_weight, read_weight):
    members, nodes = acc.shape
    feats = read_weight.shape[1]
    half = feats // LONC
    out_shape = (
        jax.ShapeDtypeStruct((members, feats), jnp.float32),
        jax.ShapeDtypeStruct((members, feats), jnp.bfloat16),
        jax.ShapeDtypeStruct((members, half), jnp.bfloat16),
        jax.ShapeDtypeStruct((members, half), jnp.bfloat16),
        jax.ShapeDtypeStruct((members, nodes), jnp.bfloat16),
    )
    return pl.pallas_call(
        step_kernel,
        out_shape=out_shape,
        in_specs=[pl.BlockSpec(memory_space=pltpu.MemorySpace.SMEM)] + [VMEM_SPEC] * 9,
        out_specs=tuple([VMEM_SPEC] * 5),
        scratch_shapes=[pltpu.VMEM((members, nodes), jnp.bfloat16)],
        compiler_params=pltpu.CompilerParams(vmem_limit_bytes=32 * 1024 * 1024),
    )(flags, acc, lon_a, lon_b, lat_a, lat_b, sel_n, sel_s, entry_weight, read_weight)


def swaps(peers, odd_first, wrap):
    pairs = []
    for i in range(peers):
        partner = i + 1 if (i % 2 == 1) == odd_first else i - 1
        if wrap:
            partner %= peers
        if 0 <= partner < peers:
            pairs.append((i, partner))
    return pairs


def per_device(initial_state, initial_reservoir, coupling, input_weight, readout, intersection):
    current = initial_state[0, 0]
    reservoir = initial_reservoir[0, 0]
    block_weight = coupling[0, 0]
    entry_weight = input_weight[0, 0]
    read_weight = readout[0, 0]
    lists = intersection[0, 0]
    half = current.shape[1] // LONC
    lon_even = (lax.axis_index("lon") % 2 == 0).astype(jnp.int32)
    lat_even = (lax.axis_index("lat") % 2 == 0).astype(jnp.int32)
    flags = jnp.stack([lon_even, lat_even])
    lon_peers = lax.axis_size("lon")
    lat_peers = lax.axis_size("lat")
    lon_pairs_a = swaps(lon_peers, False, True)
    lon_pairs_b = swaps(lon_peers, True, True)
    lat_pairs_a = swaps(lat_peers, False, False)
    lat_pairs_b = swaps(lat_peers, True, False)
    rounded = current.astype(jnp.bfloat16)
    low = rounded[:, :half]
    high = rounded[:, half:]
    send_a = jnp.where(lon_even == 1, high, low)
    send_b = jnp.where(lon_even == 1, low, high)
    outputs = []
    for _ in range(STEPS):
        lon_b = lax.ppermute(send_b, "lon", lon_pairs_b)
        lon_a = lax.ppermute(send_a, "lon", lon_pairs_a)
        lat_b = lax.ppermute(rounded, "lat", lat_pairs_b)
        lat_a = lax.ppermute(rounded, "lat", lat_pairs_a)
        acc, sel_n, sel_s = couple_call(lists, rounded, reservoir, block_weight, entry_weight)
        current, rounded, send_a, send_b, reservoir = step_call(
            flags, acc, lon_a, lon_b, lat_a, lat_b, sel_n, sel_s, entry_weight, read_weight)
        outputs.append(current)
    return jnp.stack(outputs)[:, None, None]


def solution(mesh):
    in_specs = (
        P("lat", "lon", None, None),
        P("lat", "lon", None, None),
        P("lat", "lon", None, None, None, None),
        P("lat", "lon", None, None, None),
        P("lat", "lon", None, None),
        P("lat", "lon", None, None),
    )
    out_specs = P(None, "lat", "lon", None, None)
    return jax.shard_map(
        per_device, mesh=mesh, in_specs=in_specs, out_specs=out_specs, check_vma=False
    )
```
